128 devices in a mesh: occ: 16 (over z, x_lo, core), aux: 8 (over y, x_hi).
Axes of the slice: x: 4 (x_hi: 2, x_lo: 2; x = x_hi * 2 + x_lo), y: 4, z: 4, core: 2. Of those that a mesh axis runs over, the one named last changes fastest.
Arguments:
- integrals: bfloat16 [11264, 16, 2176], P(('occ', 'aux')), may hold values from -0.5 to 0.5
- owner_order: int32 [16], replicated, may hold values from 0 to 15, each once
- occ_energy: float32 [16], replicated, may hold values from -1.5 to -0.3
- vir_energy: float32 [2176], replicated, may hold values from 0.03 to 30
Outputs:
- pair_rows: float32 [16, 1, 2176], P('occ', None, 'aux')
- pair_energy: float32 [16, 1], P('occ')
The draws below stay inside these ranges and needn't reach their ends.
Inputs may be any that keep to these rules, and one draw needn't show every extreme that they name: owner_order holds each of 0 to 15 once; only its first 1 entries are used.
All inputs are finite; a program needn't handle non-finite values.
Results may differ from the reference program's by a relative error of at most 0.0003.
Values may be sent and summed in bfloat16 or wider, within the bound.
No kernel may reach another device: no remote copies, remote signals or barrier semaphores. Data moves between devices by JAX's collectives and lax.ppermute only.
A program may use at most 128 MiB of HBM per device.

```python
import math
import jax
import jax.numpy as jnp
from jax import lax

NAUX = 11264
NVIR = 2176
STEPS = 1
NOCC_W = 16
QROW = 88
N_OCC = 16
N_AUX = 8


def draw_vir_energy(key, part):
    position = jnp.arange(NVIR, dtype=jnp.float32) / (NVIR - 1)
    base_level = 0.05 * jnp.exp(position * math.log(400.0))
    factor = jax.random.uniform(key, (NVIR,), jnp.float32, 0.8, 1.25)
    return base_level * factor


def with_spikes(array, key, source, target, shards_of, factor):
    owner, partner = [(jnp.arange(array.shape[dim]) // (array.shape[dim] // shards_of)).reshape([-1 if axis == dim else 1 for axis in range(array.ndim)]) for dim in (source, target)]
    chosen = jax.random.permutation(key, shards_of)[partner]
    strong = (owner == chosen) | (owner == (partner + shards_of // 2) % shards_of)
    return jnp.where(strong, factor * array, array)


def steps_of(key, extent, shards, least, top_value):
    def one(dim, blocks):
        steps = jax.random.uniform(jax.random.fold_in(jax.random.fold_in(key, 6), dim), (blocks,), jnp.float32, least / len(shards), top_value / len(shards))
        return jnp.repeat(jnp.exp(steps), extent[dim] // blocks).reshape((-1,) + (1,) * (len(extent) - dim - 1))

    level = one(*shards[0])
    for cut in shards[1:]:
        level = level * one(*cut)
    return level


def bell_draw_with(own_key, dims, scale, limit, cuts, heavy, held_as=jnp.bfloat16):
    result = scale * jax.random.normal(own_key, dims, jnp.float32)
    if cuts:
        result = result * steps_of(own_key, dims, cuts, -0.22, 0.18)
    return jnp.clip(with_spikes(result, jax.random.fold_in(own_key, 3), *heavy), -limit, limit).astype(held_as)


def setup_inputs(seed: int = 0) -> dict:
    splits = jax.random.split(jax.random.key(seed), 5)
    integrals = bell_draw_with(splits[0], (NAUX, NOCC_W, NVIR), (1.5 * (NAUX * NVIR) ** -0.25), 0.5, ((0, 128),), (0, 2, 128, 5.5))
    owner_order = jax.random.permutation(splits[1], N_OCC).astype(jnp.int32)
    occ_energy = jnp.clip(jax.random.uniform(splits[2], (NOCC_W,), jnp.float32, -1.5, -0.3), -1.5, -0.3)
    vir_energy = draw_vir_energy(jax.random.fold_in(splits[4], 71), 0)
    return dict(integrals=integrals, owner_order=owner_order, occ_energy=occ_energy, vir_energy=vir_energy)


def reference(integrals, owner_order, occ_energy, vir_energy):
    grouped = integrals.reshape(N_OCC, N_AUX, QROW, NOCC_W, NVIR)

    def orbital_rows(orbital):
        left_rows = lax.dynamic_index_in_dim(grouped, orbital, 3, keepdims=False).astype(jnp.float32)
        own_energy = lax.dynamic_index_in_dim(occ_energy, orbital, 0, keepdims=False)
        results = []
        for window_step in range(STEPS):
            owner = owner_order[window_step]
            right_rows = lax.dynamic_index_in_dim(grouped, owner, 3, keepdims=False).astype(jnp.float32)
            partial_sum = jnp.einsum("oxqa,oxqb->xab", left_rows, right_rows)
            coupling = jnp.sum(partial_sum, axis=0)
            owner_energy = lax.dynamic_index_in_dim(occ_energy, owner, 0, keepdims=False)
            denominator = own_energy + owner_energy - vir_energy[:, None] - vir_energy[None, :]
            results.append(jnp.sum(coupling * coupling / denominator, axis=1))
        return jnp.stack(results, axis=0)

    pair_rows = lax.map(orbital_rows, jnp.arange(NOCC_W, dtype=jnp.int32))
    return pair_rows, jnp.sum(pair_rows, axis=2)
```

```python
import jax
import jax.numpy as jnp
from jax import lax
from jax.sharding import Mesh, PartitionSpec as P

GROUP = ("oz", "core", "xh")


def per_device(integrals, owner_order, occ_energy, vir_energy):
    nq, nocc, nvir = integrals.shape
    ny, nh, nc = lax.axis_size("y"), lax.axis_size("xh"), lax.axis_size("core")
    noz = lax.axis_size("oz")
    blk = nvir // (ny * nh)
    y, h, c = lax.axis_index("y"), lax.axis_index("xh"), lax.axis_index("core")
    orbital = lax.axis_index("oz") * nc + c

    tiles = integrals.reshape(nq, nocc, ny, nh, blk)
    tiles = jnp.transpose(tiles, (1, 3, 0, 2, 4)).reshape(nocc * nh, nq, ny * blk)
    left = lax.all_to_all(tiles, GROUP, 0, 0, tiled=True)
    left = left.reshape(noz, nc, nh, nq, ny * blk)

    owner = owner_order[0]
    column = lax.dynamic_index_in_dim(integrals, owner, 1, keepdims=False)
    chip_rows = lax.all_gather(column, "core", axis=0, tiled=False)
    half = nvir // nc
    mine = lax.dynamic_slice_in_dim(chip_rows, c * half, half, axis=2)
    panel = lax.all_gather(mine, ("oz", "xh"), axis=0, tiled=False)
    panel = panel.reshape(noz, nh, nc, nq, half)
    panel = lax.all_gather(panel, "core", axis=0, tiled=False)

    partial_sum = lax.dot_general(
        left, panel, (((0, 1, 2, 3), (1, 3, 2, 4)), ((), ())), preferred_element_type=jnp.float32
    ).reshape(ny * blk, nvir)
    summed = lax.psum_scatter(partial_sum, "y", scatter_dimension=0, tiled=True)

    near_energy = lax.dynamic_slice_in_dim(vir_energy, (y * nh + h) * blk, blk)
    own_energy = lax.dynamic_index_in_dim(occ_energy, orbital, 0, keepdims=False)
    owner_energy = lax.dynamic_index_in_dim(occ_energy, owner, 0, keepdims=False)
    denominator = own_energy + owner_energy - near_energy[:, None] - vir_energy[None, :]
    rows = jnp.sum(summed * summed / denominator, axis=1)
    pair_rows = rows.reshape(1, 1, blk)
    totals = lax.psum(jnp.sum(rows), ("y", "xh")).reshape(1, 1)
    return pair_rows, totals


def solution(mesh):
    nocc, naux = mesh.shape["occ"], mesh.shape["aux"]
    cores, ys = 2, naux // 2
    fine = Mesh(mesh.devices.reshape(nocc // cores, cores, ys, naux // ys), ("oz", "core", "y", "xh"))
    in_specs = (P(("oz", "core", "y", "xh"), None, None), P(), P(), P())
    out_specs = (P(("oz", "core"), None, ("y", "xh")), P(("oz", "core"), None))
    return jax.shard_map(
        per_device, mesh=fine, in_specs=in_specs, out_specs=out_specs, check_vma=False
    )
```

```python
import jax
import jax.numpy as jnp
from jax import lax
from jax.sharding import Mesh, PartitionSpec as P

GROUP = ("oz", "xh")


def per_device(integrals, owner_order, occ_energy, vir_energy):
    nq, nocc, nvir = integrals.shape
    ny, nh, nc = lax.axis_size("y"), lax.axis_size("xh"), lax.axis_size("core")
    blk = nvir // (ny * nh)
    oz, y, h, c = lax.axis_index("oz"), lax.axis_index("y"), lax.axis_index("xh"), lax.axis_index("core")
    orbital = oz * nh + h

    left = lax.all_to_all(integrals, GROUP, 1, 0, tiled=True)[:, 0, :]
    owner = owner_order[0]
    column = lax.dynamic_index_in_dim(integrals, owner, 1, keepdims=False)
    panel = lax.all_gather(column, GROUP, axis=0, tiled=True)

    left = jnp.transpose(left.reshape(-1, ny, nc, blk), (0, 2, 1, 3))
    partial_sum = lax.dot_general(
        left, panel, (((0,), (0,)), ((), ())), preferred_element_type=jnp.float32
    ).reshape(nc * ny * blk, nvir)
    summed = lax.psum_scatter(partial_sum, "core", scatter_dimension=0, tiled=True)
    summed = lax.psum_scatter(summed, "y", scatter_dimension=0, tiled=True)

    near_energy = lax.dynamic_slice_in_dim(vir_energy, (y * nc + c) * blk, blk)
    own_energy = lax.dynamic_index_in_dim(occ_energy, orbital, 0, keepdims=False)
    owner_energy = lax.dynamic_index_in_dim(occ_energy, owner, 0, keepdims=False)
    denominator = own_energy + owner_energy - near_energy[:, None] - vir_energy[None, :]
    rows = jnp.sum(summed * summed / denominator, axis=1)

    swap = [(cc * nh + hh, hh * nc + cc) for cc in range(nc) for hh in range(nh)]
    rows = lax.ppermute(rows, ("core", "xh"), swap)
    totals = lax.psum(jnp.sum(rows), ("y", "xh")).reshape(1, 1)
    return rows.reshape(1, 1, blk), totals


def solution(mesh):
    nocc, naux = mesh.shape["occ"], mesh.shape["aux"]
    cores, ys = 2, naux // 2
    fine = Mesh(mesh.devices.reshape(nocc // cores, cores, ys, naux // ys), ("oz", "core", "y", "xh"))
    in_specs = (P(("oz", "core", "y", "xh"), None, None), P(), P(), P())
    out_specs = (P(("oz", "core"), None, ("y", "xh")), P(("oz", "core"), None))
    return jax.shard_map(
        per_device, mesh=fine, in_specs=in_specs, out_specs=out_specs, check_vma=False
    )
```

```python
import jax
import jax.numpy as jnp
from jax import lax
from jax.sharding import Mesh, PartitionSpec as P

GROUP = ("z", "xh", "xl")


def per_device(integrals, owner_order, occ_energy, vir_energy):
    nq, nocc, nvir = integrals.shape
    ny, nh, nc, nl = lax.axis_size("y"), lax.axis_size("xh"), lax.axis_size("core"), lax.axis_size("xl")
    blk = nvir // (ny * nh)
    z, l, y, h, c = (lax.axis_index(a) for a in ("z", "xl", "y", "xh", "core"))
    orbital = (z * nh + h) * nl + l
    block = c * ny + y

    left = lax.all_to_all(integrals, GROUP, 1, 0, tiled=True)[:, 0, :]
    owner = owner_order[0]
    column = lax.dynamic_index_in_dim(integrals, owner, 1, keepdims=False)
    panel = lax.all_gather(column, GROUP, axis=0, tiled=True)

    partial_sum = lax.dot_general(
        left, panel, (((0,), (0,)), ((), ())), preferred_element_type=jnp.float32
    )
    summed = lax.psum_scatter(partial_sum, "core", scatter_dimension=0, tiled=True)
    summed = lax.psum_scatter(summed, "y", scatter_dimension=0, tiled=True)

    near_energy = lax.dynamic_slice_in_dim(vir_energy, block * blk, blk)
    own_energy = lax.dynamic_index_in_dim(occ_energy, orbital, 0, keepdims=False)
    owner_energy = lax.dynamic_index_in_dim(occ_energy, owner, 0, keepdims=False)
    denominator = own_energy + owner_energy - near_energy[:, None] - vir_energy[None, :]
    rows = jnp.sum(summed * summed / denominator, axis=1)

    total = jnp.sum(rows)
    total = total + lax.ppermute(total, "core", [(k, (k + 1) % nc) for k in range(nc)])
    total = total + lax.ppermute(total, "y", [(k, (k + 1) % ny) for k in range(ny)])
    total = total + lax.ppermute(total, "y", [(k, (k + 2) % ny) for k in range(ny)])

    def index(ll, cc, yy, hh):
        return ((ll * nc + cc) * ny + yy) * nh + hh

    moves = []
    for ll in range(nl):
        for cc in range(nc):
            for yy in range(ny):
                for hh in range(nh):
                    b = cc * ny + yy
                    moves.append((index(ll, cc, yy, hh), index(hh, ll, b // nh, b % nh)))
    packed = jnp.concatenate([rows, total[None]])
    packed = lax.ppermute(packed, ("xl", "core", "y", "xh"), moves)
    return packed[:blk].reshape(1, 1, blk), packed[blk:].reshape(1, 1)


def solution(mesh):
    nocc, naux = mesh.shape["occ"], mesh.shape["aux"]
    cores, xls, ys = 2, 2, naux // 2
    shape = (nocc // (cores * xls), xls, cores, ys, naux // ys)
    fine = Mesh(mesh.devices.reshape(shape), ("z", "xl", "core", "y", "xh"))
    in_specs = (P(("z", "xl", "core", "y", "xh"), None, None), P(), P(), P())
    out_specs = (P(("z", "xl", "core"), None, ("y", "xh")), P(("z", "xl", "core"), None))
    return jax.shard_map(
        per_device, mesh=fine, in_specs=in_specs, out_specs=out_specs, check_vma=False
    )
```

```python
import jax
import jax.numpy as jnp
from jax import lax
from jax.sharding import Mesh, PartitionSpec as P

GROUP = ("z", "xh", "xl")


def per_device(integrals, owner_order, occ_energy, vir_energy):
    nq, nocc, nvir = integrals.shape
    ny, nh, nc, nl = lax.axis_size("y"), lax.axis_size("xh"), lax.axis_size("core"), lax.axis_size("xl")
    blk = nvir // (ny * nh)
    z, l, y, h, c = (lax.axis_index(a) for a in ("z", "xl", "y", "xh", "core"))
    orbital = (z * nh + h) * nl + l
    block = c * ny + y

    left = lax.all_to_all(integrals, GROUP, 1, 0, tiled=True)[:, 0, :]
    owner = owner_order[0]
    column = lax.dynamic_index_in_dim(integrals, owner, 1, keepdims=False)
    panel = lax.all_gather(column, GROUP, axis=0, tiled=True)

    partial_sum = lax.dot_general(
        left, panel, (((0,), (0,)), ((), ())), preferred_element_type=jnp.float32
    )
    summed = lax.psum_scatter(partial_sum, "core", scatter_dimension=1, tiled=True)
    summed = lax.psum_scatter(summed, "y", scatter_dimension=1, tiled=True)

    near_energy = lax.dynamic_slice_in_dim(vir_energy, block * blk, blk)
    own_energy = lax.dynamic_index_in_dim(occ_energy, orbital, 0, keepdims=False)
    owner_energy = lax.dynamic_index_in_dim(occ_energy, owner, 0, keepdims=False)
    denominator = own_energy + owner_energy - vir_energy[:, None] - near_energy[None, :]
    part_rows = jnp.sum(summed * summed / denominator, axis=1)

    total = jnp.sum(part_rows)
    pieces = part_rows.reshape(nc, ny // 2, 2, blk)
    for axis, bit, step, size in (("core", c, 1, nc), ("y", y // 2, 2, ny), ("y", y % 2, 1, ny)):
        keep = lax.dynamic_index_in_dim(pieces, bit, 0, keepdims=False)
        give = lax.dynamic_index_in_dim(pieces, 1 - bit, 0, keepdims=False)
        flip = [(k, k ^ step) for k in range(size)]
        got = lax.ppermute(jnp.concatenate([give.reshape(-1), total[None]]), axis, flip)
        pieces = keep + got[:-1].reshape(keep.shape)
        total = total + got[-1]
    rows = pieces.reshape(blk)

    def index(ll, cc, yy, hh):
        return ((ll * nc + cc) * ny + yy) * nh + hh

    moves = []
    for ll in range(nl):
        for cc in range(nc):
            for yy in range(ny):
                for hh in range(nh):
                    b = cc * ny + yy
                    moves.append((index(ll, cc, yy, hh), index(hh, ll, b // nh, b % nh)))
    packed = jnp.concatenate([rows, total[None]])
    packed = lax.ppermute(packed, ("xl", "core", "y", "xh"), moves)
    return packed[:blk].reshape(1, 1, blk), packed[blk:].reshape(1, 1)


def solution(mesh):
    nocc, naux = mesh.shape["occ"], mesh.shape["aux"]
    cores, xls, ys = 2, 2, naux // 2
    shape = (nocc // (cores * xls), xls, cores, ys, naux // ys)
    fine = Mesh(mesh.devices.reshape(shape), ("z", "xl", "core", "y", "xh"))
    in_specs = (P(("z", "xl", "core", "y", "xh"), None, None), P(), P(), P())
    out_specs = (P(("z", "xl", "core"), None, ("y", "xh")), P(("z", "xl", "core"), None))
    return jax.shard_map(
        per_device, mesh=fine, in_specs=in_specs, out_specs=out_specs, check_vma=False
    )
```

```python
import jax
import jax.numpy as jnp
from jax import lax
from jax.sharding import Mesh, PartitionSpec as P

GROUP = ("z", "xh", "xl")


def per_device(integrals, owner_order, occ_energy, vir_energy):
    nq, nocc, nvir = integrals.shape
    ny, nh, nc, nl = lax.axis_size("y"), lax.axis_size("xh"), lax.axis_size("core"), lax.axis_size("xl")
    blk = nvir // (ny * nh)
    z, l, y, h, c = (lax.axis_index(a) for a in ("z", "xl", "y", "xh", "core"))
    orbital = (z * nh + h) * nl + l
    block = c * ny + y

    left = lax.all_to_all(integrals, GROUP, 1, 0, tiled=True)[:, 0, :]
    owner = owner_order[0]
    column = lax.dynamic_index_in_dim(integrals, owner, 1, keepdims=False)
    panel = lax.all_gather(column, GROUP, axis=0, tiled=True)

    partial_sum = lax.dot_general(
        left, panel, (((0,), (0,)), ((), ())), preferred_element_type=jnp.float32
    )
    summed = lax.psum_scatter(partial_sum, "core", scatter_dimension=1, tiled=True)
    summed = lax.psum_scatter(summed, "y", scatter_dimension=1, tiled=True)

    near_energy = lax.dynamic_slice_in_dim(vir_energy, block * blk, blk)
    own_energy = lax.dynamic_index_in_dim(occ_energy, orbital, 0, keepdims=False)
    owner_energy = lax.dynamic_index_in_dim(occ_energy, owner, 0, keepdims=False)
    denominator = own_energy + owner_energy - vir_energy[:, None] - near_energy[None, :]
    part_rows = jnp.sum(summed * summed / denominator, axis=1)

    nb = nc * ny
    part_total = jnp.sum(part_rows)

    def index(ll, cc, yy, hh):
        return ((ll * nc + cc) * ny + yy) * nh + hh

    got = []
    for k in range(nb):
        moves = []
        for ll in range(nl):
            for cc in range(nc):
                for yy in range(ny):
                    for hh in range(nh):
                        x = (cc * ny + yy + k) % nb
                        moves.append((index(ll, cc, yy, hh), index(hh, ll, x // nh, x % nh)))
        piece = lax.dynamic_slice_in_dim(part_rows, ((block + k) % nb) * blk, blk)
        packed = jnp.concatenate([piece, part_total[None]])
        got.append(lax.ppermute(packed, ("xl", "core", "y", "xh"), moves))
    packed = sum(got[1:], got[0])
    return packed[:blk].reshape(1, 1, blk), packed[blk:].reshape(1, 1)


def solution(mesh):
    nocc, naux = mesh.shape["occ"], mesh.shape["aux"]
    cores, xls, ys = 2, 2, naux // 2
    shape = (nocc // (cores * xls), xls, cores, ys, naux // ys)
    fine = Mesh(mesh.devices.reshape(shape), ("z", "xl", "core", "y", "xh"))
    in_specs = (P(("z", "xl", "core", "y", "xh"), None, None), P(), P(), P())
    out_specs = (P(("z", "xl", "core"), None, ("y", "xh")), P(("z", "xl", "core"), None))
    return jax.shard_map(
        per_device, mesh=fine, in_specs=in_specs, out_specs=out_specs, check_vma=False
    )
```

```python
import jax
import jax.numpy as jnp
from jax import lax
from jax.sharding import Mesh, PartitionSpec as P

GROUP = ("z", "xh", "xl")
CHUNKS = 2


def per_device(integrals, owner_order, occ_energy, vir_energy):
    nq, nocc, nvir = integrals.shape
    ny, nh, nc, nl = lax.axis_size("y"), lax.axis_size("xh"), lax.axis_size("core"), lax.axis_size("xl")
    blk = nvir // (ny * nh)
    z, l, y, h, c = (lax.axis_index(a) for a in ("z", "xl", "y", "xh", "core"))
    orbital = (z * nh + h) * nl + l
    block = c * ny + y

    left = lax.all_to_all(integrals, GROUP, 1, 0, tiled=True)[:, 0, :]
    owner = owner_order[0]
    column = lax.dynamic_index_in_dim(integrals, owner, 1, keepdims=False)
    panel = lax.all_gather(column, GROUP, axis=0, tiled=True)

    near_energy = lax.dynamic_slice_in_dim(vir_energy, block * blk, blk)
    own_energy = lax.dynamic_index_in_dim(occ_energy, orbital, 0, keepdims=False)
    owner_energy = lax.dynamic_index_in_dim(occ_energy, owner, 0, keepdims=False)
    half = nvir // nc
    flip = [(k, k ^ 1) for k in range(nc)]

    lanes = nvir // 128
    cuts = [0] + [lanes * k // CHUNKS * 128 for k in range(1, CHUNKS)] + [nvir]
    part_rows = []
    for lo, hi in zip(cuts[:-1], cuts[1:]):
        partial_sum = lax.dot_general(
            left[:, lo:hi], panel, (((0,), (0,)), ((), ())), preferred_element_type=jnp.float32
        )
        keep = lax.dynamic_slice_in_dim(partial_sum, c * half, half, axis=1)
        give = lax.dynamic_slice_in_dim(partial_sum, (1 - c) * half, half, axis=1)
        summed = keep + lax.ppermute(give, "core", flip)
        summed = lax.psum_scatter(summed, "y", scatter_dimension=1, tiled=True)
        denominator = own_energy + owner_energy - vir_energy[lo:hi, None] - near_energy[None, :]
        part_rows.append(jnp.sum(summed * summed / denominator, axis=1))
    part_rows = jnp.concatenate(part_rows)

    total = jnp.sum(part_rows)
    pieces = part_rows.reshape(nc, ny // 2, 2, blk)
    for axis, bit, step, size in (("core", c, 1, nc), ("y", y // 2, 2, ny), ("y", y % 2, 1, ny)):
        keep = lax.dynamic_index_in_dim(pieces, bit, 0, keepdims=False)
        give = lax.dynamic_index_in_dim(pieces, 1 - bit, 0, keepdims=False)
        flip = [(k, k ^ step) for k in range(size)]
        got = lax.ppermute(jnp.concatenate([give.reshape(-1), total[None]]), axis, flip)
        pieces = keep + got[:-1].reshape(keep.shape)
        total = total + got[-1]
    rows = pieces.reshape(blk)

    def index(ll, cc, yy, hh):
        return ((ll * nc + cc) * ny + yy) * nh + hh

    moves = []
    for ll in range(nl):
        for cc in range(nc):
            for yy in range(ny):
                for hh in range(nh):
                    b = cc * ny + yy
                    moves.append((index(ll, cc, yy, hh), index(hh, ll, b // nh, b % nh)))
    packed = jnp.concatenate([rows, total[None]])
    packed = lax.ppermute(packed, ("xl", "core", "y", "xh"), moves)
    return packed[:blk].reshape(1, 1, blk), packed[blk:].reshape(1, 1)


def solution(mesh):
    nocc, naux = mesh.shape["occ"], mesh.shape["aux"]
    cores, xls, ys = 2, 2, naux // 2
    shape = (nocc // (cores * xls), xls, cores, ys, naux // ys)
    fine = Mesh(mesh.devices.reshape(shape), ("z", "xl", "core", "y", "xh"))
    in_specs = (P(("z", "xl", "core", "y", "xh"), None, None), P(), P(), P())
    out_specs = (P(("z", "xl", "core"), None, ("y", "xh")), P(("z", "xl", "core"), None))
    return jax.shard_map(
        per_device, mesh=fine, in_specs=in_specs, out_specs=out_specs, check_vma=False
    )
```

```python
import jax
import jax.numpy as jnp
from jax import lax
from jax.sharding import Mesh, PartitionSpec as P

GROUP = ("z", "xh", "xl")


def per_device(integrals, owner_order, occ_energy, vir_energy):
    nq, nocc, nvir = integrals.shape
    ny, nh, nc, nl = lax.axis_size("y"), lax.axis_size("xh"), lax.axis_size("core"), lax.axis_size("xl")
    blk = nvir // (ny * nh)
    z, l, y, h, c = (lax.axis_index(a) for a in ("z", "xl", "y", "xh", "core"))
    orbital = (z * nh + h) * nl + l
    block = c * ny + y

    owner = owner_order[0]
    column = lax.dynamic_index_in_dim(integrals, owner, 1, keepdims=False)
    column, integrals = lax.optimization_barrier((column, integrals))
    panel = lax.all_gather(column, GROUP, axis=0, tiled=True)
    left = lax.all_to_all(integrals, GROUP, 1, 0, tiled=True)[:, 0, :]

    partial_sum = lax.dot_general(
        left, panel, (((0,), (0,)), ((), ())), preferred_element_type=jnp.float32
    )
    summed = lax.psum_scatter(partial_sum, "core", scatter_dimension=1, tiled=True)
    summed = lax.psum_scatter(summed, "y", scatter_dimension=1, tiled=True)

    near_energy = lax.dynamic_slice_in_dim(vir_energy, block * blk, blk)
    own_energy = lax.dynamic_index_in_dim(occ_energy, orbital, 0, keepdims=False)
    owner_energy = lax.dynamic_index_in_dim(occ_energy, owner, 0, keepdims=False)
    denominator = own_energy + owner_energy - vir_energy[:, None] - near_energy[None, :]
    part_rows = jnp.sum(summed * summed / denominator, axis=1)

    total = jnp.sum(part_rows)
    pieces = part_rows.reshape(nc, ny // 2, 2, blk)
    for axis, bit, step, size in (("core", c, 1, nc), ("y", y // 2, 2, ny), ("y", y % 2, 1, ny)):
        keep = lax.dynamic_index_in_dim(pieces, bit, 0, keepdims=False)
        give = lax.dynamic_index_in_dim(pieces, 1 - bit, 0, keepdims=False)
        flip = [(k, k ^ step) for k in range(size)]
        got = lax.ppermute(jnp.concatenate([give.reshape(-1), total[None]]), axis, flip)
        pieces = keep + got[:-1].reshape(keep.shape)
        total = total + got[-1]
    rows = pieces.reshape(blk)

    def index(ll, cc, yy, hh):
        return ((ll * nc + cc) * ny + yy) * nh + hh

    moves = []
    for ll in range(nl):
        for cc in range(nc):
            for yy in range(ny):
                for hh in range(nh):
                    b = cc * ny + yy
                    moves.append((index(ll, cc, yy, hh), index(hh, ll, b // nh, b % nh)))
    packed = jnp.concatenate([rows, total[None]])
    packed = lax.ppermute(packed, ("xl", "core", "y", "xh"), moves)
    return packed[:blk].reshape(1, 1, blk), packed[blk:].reshape(1, 1)


def solution(mesh):
    nocc, naux = mesh.shape["occ"], mesh.shape["aux"]
    cores, xls, ys = 2, 2, naux // 2
    shape = (nocc // (cores * xls), xls, cores, ys, naux // ys)
    fine = Mesh(mesh.devices.reshape(shape), ("z", "xl", "core", "y", "xh"))
    in_specs = (P(("z", "xl", "core", "y", "xh"), None, None), P(), P(), P())
    out_specs = (P(("z", "xl", "core"), None, ("y", "xh")), P(("z", "xl", "core"), None))
    return jax.shard_map(
        per_device, mesh=fine, in_specs=in_specs, out_specs=out_specs, check_vma=False
    )
```

```python
import jax
import jax.numpy as jnp
from jax import lax
from jax.sharding import Mesh, PartitionSpec as P

GROUP = ("z", "xh", "xl")


def per_device(integrals, owner_order, occ_energy, vir_energy):
    nq, nocc, nvir = integrals.shape
    ny, nh, nc, nl = lax.axis_size("y"), lax.axis_size("xh"), lax.axis_size("core"), lax.axis_size("xl")
    blk = nvir // (ny * nh)
    z, l, y, h, c = (lax.axis_index(a) for a in ("z", "xl", "y", "xh", "core"))
    orbital = (z * nh + h) * nl + l
    block = c * ny + y

    owner = owner_order[0]
    half = nvir // nc
    flip = [(k, k ^ 1) for k in range(nc)]
    column = lax.dynamic_index_in_dim(integrals, owner, 1, keepdims=False)
    column, integrals = lax.optimization_barrier((column, integrals))
    chip_rows = jnp.stack([column, lax.ppermute(column, "core", flip)])
    mine = lax.dynamic_slice_in_dim(chip_rows, c * half, half, axis=2)
    panel = lax.all_gather(mine, GROUP, axis=1, tiled=True).reshape(-1, half)

    left = lax.all_to_all(integrals, GROUP, 1, 0, tiled=True)[:, 0, :]
    left = jnp.concatenate([left, lax.ppermute(left, "core", flip)])

    partial_sum = lax.dot_general(
        left, panel, (((0,), (0,)), ((), ())), preferred_element_type=jnp.float32
    )
    summed = lax.psum_scatter(partial_sum, "y", scatter_dimension=1, tiled=True)

    near_energy = lax.dynamic_slice_in_dim(vir_energy, block * blk, blk)
    own_energy = lax.dynamic_index_in_dim(occ_energy, orbital, 0, keepdims=False)
    owner_energy = lax.dynamic_index_in_dim(occ_energy, owner, 0, keepdims=False)
    denominator = own_energy + owner_energy - vir_energy[:, None] - near_energy[None, :]
    part_rows = jnp.sum(summed * summed / denominator, axis=1)

    total = jnp.sum(part_rows)
    pieces = part_rows.reshape(nc, ny // 2, 2, blk)
    for axis, bit, step, size in (("core", c, 1, nc), ("y", y // 2, 2, ny), ("y", y % 2, 1, ny)):
        keep = lax.dynamic_index_in_dim(pieces, bit, 0, keepdims=False)
        give = lax.dynamic_index_in_dim(pieces, 1 - bit, 0, keepdims=False)
        flip = [(k, k ^ step) for k in range(size)]
        got = lax.ppermute(jnp.concatenate([give.reshape(-1), total[None]]), axis, flip)
        pieces = keep + got[:-1].reshape(keep.shape)
        total = total + got[-1]
    rows = pieces.reshape(blk)

    def index(ll, cc, yy, hh):
        return ((ll * nc + cc) * ny + yy) * nh + hh

    moves = []
    for ll in range(nl):
        for cc in range(nc):
            for yy in range(ny):
                for hh in range(nh):
                    b = cc * ny + yy
                    moves.append((index(ll, cc, yy, hh), index(hh, ll, b // nh, b % nh)))
    packed = jnp.concatenate([rows, total[None]])
    packed = lax.ppermute(packed, ("xl", "core", "y", "xh"), moves)
    return packed[:blk].reshape(1, 1, blk), packed[blk:].reshape(1, 1)


def solution(mesh):
    nocc, naux = mesh.shape["occ"], mesh.shape["aux"]
    cores, xls, ys = 2, 2, naux // 2
    shape = (nocc // (cores * xls), xls, cores, ys, naux // ys)
    fine = Mesh(mesh.devices.reshape(shape), ("z", "xl", "core", "y", "xh"))
    in_specs = (P(("z", "xl", "core", "y", "xh"), None, None), P(), P(), P())
    out_specs = (P(("z", "xl", "core"), None, ("y", "xh")), P(("z", "xl", "core"), None))
    return jax.shard_map(
        per_device, mesh=fine, in_specs=in_specs, out_specs=out_specs, check_vma=False
    )
```

```python
import jax
import jax.numpy as jnp
from jax import lax
from jax.sharding import Mesh, PartitionSpec as P

GROUP = ("z", "xh", "xl")


def body(integrals, owner_order, occ_energy, vir_energy):
    _, _, nvir = integrals.shape
    ny, nh, nc, nl = lax.axis_size("y"), lax.axis_size("xh"), lax.axis_size("core"), lax.axis_size("xl")
    blk = nvir // (ny * nh)
    z, l, y, h, c = (lax.axis_index(a) for a in ("z", "xl", "y", "xh", "core"))
    orbital = (z * nh + h) * nl + l
    block = c * ny + y

    owner = owner_order[0]
    half = nvir // nc
    flip = [(k, k ^ 1) for k in range(nc)]
    column = lax.dynamic_index_in_dim(integrals, owner, 1, keepdims=False)
    chip_rows = jnp.stack([column, lax.ppermute(column, "core", flip)])
    mine = lax.dynamic_slice_in_dim(chip_rows, c * half, half, axis=2)
    mine, integrals = lax.optimization_barrier((mine, integrals))
    by_orbital = jnp.transpose(integrals, (1, 0, 2))
    panel = lax.all_gather(mine, GROUP, axis=1, tiled=True)
    panel = panel.reshape(-1, half)

    left = lax.all_to_all(by_orbital, GROUP, 0, 0, tiled=True)
    left = left.reshape(-1, nvir)
    left = jnp.concatenate([left, lax.ppermute(left, "core", flip)])

    partial_sum = lax.dot_general(
        left, panel, (((0,), (0,)), ((), ())), preferred_element_type=jnp.float32
    )
    summed = lax.psum_scatter(partial_sum, "y", scatter_dimension=1, tiled=True)

    near_energy = lax.dynamic_slice_in_dim(vir_energy, block * blk, blk)
    own_energy = lax.dynamic_index_in_dim(occ_energy, orbital, 0, keepdims=False)
    owner_energy = lax.dynamic_index_in_dim(occ_energy, owner, 0, keepdims=False)
    denominator = own_energy + owner_energy - vir_energy[:, None] - near_energy[None, :]
    part_rows = jnp.sum(summed * summed / denominator, axis=1)

    total = jnp.sum(part_rows)
    pieces = part_rows.reshape(nc, ny // 2, 2, blk)
    for axis, bit, step, size in (("core", c, 1, nc), ("y", y // 2, 2, ny), ("y", y % 2, 1, ny)):
        keep = lax.dynamic_index_in_dim(pieces, bit, 0, keepdims=False)
        give = lax.dynamic_index_in_dim(pieces, 1 - bit, 0, keepdims=False)
        flip = [(k, k ^ step) for k in range(size)]
        got = lax.ppermute(jnp.concatenate([give.reshape(-1), total[None]]), axis, flip)
        pieces = keep + got[:-1].reshape(keep.shape)
        total = total + got[-1]
    rows = pieces.reshape(blk)

    def index(ll, cc, yy, hh):
        return ((ll * nc + cc) * ny + yy) * nh + hh

    moves = []
    for ll in range(nl):
        for cc in range(nc):
            for yy in range(ny):
                for hh in range(nh):
                    b = cc * ny + yy
                    moves.append((index(ll, cc, yy, hh), index(hh, ll, b // nh, b % nh)))
    packed = jnp.concatenate([rows, total[None]])
    packed = lax.ppermute(packed, ("xl", "core", "y", "xh"), moves)
    return packed[:blk].reshape(1, 1, blk), packed[blk:].reshape(1, 1)


def solution(mesh):
    nocc, naux = mesh.shape["occ"], mesh.shape["aux"]
    cores, xls, ys = 2, 2, naux // 2
    shape = (nocc // (cores * xls), xls, cores, ys, naux // ys)
    fine = Mesh(mesh.devices.reshape(shape), ("z", "xl", "core", "y", "xh"))
    in_specs = (P(("z", "xl", "core", "y", "xh"), None, None), P(), P(), P())
    out_specs = (P(("z", "xl", "core"), None, ("y", "xh")), P(("z", "xl", "core"), None))
    return jax.shard_map(body, mesh=fine, in_specs=in_specs, out_specs=out_specs, check_vma=False)
```

```python
import jax
import jax.numpy as jnp
from jax import lax
from jax.sharding import Mesh, PartitionSpec as P

GROUP = ("z", "xh", "xl")


def body(integrals, owner_order, occ_energy, vir_energy):
    _, _, nvir = integrals.shape
    ny, nh, nc, nl = lax.axis_size("y"), lax.axis_size("xh"), lax.axis_size("core"), lax.axis_size("xl")
    blk = nvir // (ny * nh)
    z, l, y, h, c = (lax.axis_index(a) for a in ("z", "xl", "y", "xh", "core"))
    orbital = (z * nh + h) * nl + l
    block = c * ny + y

    owner = owner_order[0]
    half = nvir // nc
    flip = [(k, k ^ 1) for k in range(nc)]
    column = lax.dynamic_index_in_dim(integrals, owner, 1, keepdims=False)
    own_half = lax.dynamic_slice_in_dim(column, c * half, half, axis=1)
    panel_own = lax.all_gather(own_half, GROUP, axis=0, tiled=True)
    other = lax.ppermute(column, "core", flip)
    other_half = lax.dynamic_slice_in_dim(other, c * half, half, axis=1)
    panel_other = lax.all_gather(other_half, GROUP, axis=0, tiled=True)
    other_half, integrals = lax.optimization_barrier((other_half, integrals))
    by_orbital = jnp.transpose(integrals, (1, 0, 2))

    left = lax.all_to_all(by_orbital, GROUP, 0, 0, tiled=True)
    left = left.reshape(-1, nvir)
    left_other = lax.ppermute(left, "core", flip)

    contract = (((0,), (0,)), ((), ()))
    partial_sum = lax.dot_general(left, panel_own, contract, preferred_element_type=jnp.float32)
    partial_sum = partial_sum + lax.dot_general(
        left_other, panel_other, contract, preferred_element_type=jnp.float32
    )
    summed = lax.psum_scatter(partial_sum, "y", scatter_dimension=1, tiled=True)

    near_energy = lax.dynamic_slice_in_dim(vir_energy, block * blk, blk)
    own_energy = lax.dynamic_index_in_dim(occ_energy, orbital, 0, keepdims=False)
    owner_energy = lax.dynamic_index_in_dim(occ_energy, owner, 0, keepdims=False)
    denominator = own_energy + owner_energy - vir_energy[:, None] - near_energy[None, :]
    part_rows = jnp.sum(summed * summed / denominator, axis=1)

    total = jnp.sum(part_rows)
    pieces = part_rows.reshape(nc, ny // 2, 2, blk)
    for axis, bit, step, size in (("core", c, 1, nc), ("y", y // 2, 2, ny), ("y", y % 2, 1, ny)):
        keep = lax.dynamic_index_in_dim(pieces, bit, 0, keepdims=False)
        give = lax.dynamic_index_in_dim(pieces, 1 - bit, 0, keepdims=False)
        flip = [(k, k ^ step) for k in range(size)]
        got = lax.ppermute(jnp.concatenate([give.reshape(-1), total[None]]), axis, flip)
        pieces = keep + got[:-1].reshape(keep.shape)
        total = total + got[-1]
    rows = pieces.reshape(blk)

    def index(ll, cc, yy, hh):
        return ((ll * nc + cc) * ny + yy) * nh + hh

    moves = []
    for ll in range(nl):
        for cc in range(nc):
            for yy in range(ny):
                for hh in range(nh):
                    b = cc * ny + yy
                    moves.append((index(ll, cc, yy, hh), index(hh, ll, b // nh, b % nh)))
    packed = jnp.concatenate([rows, total[None]])
    packed = lax.ppermute(packed, ("xl", "core", "y", "xh"), moves)
    return packed[:blk].reshape(1, 1, blk), packed[blk:].reshape(1, 1)


def solution(mesh):
    nocc, naux = mesh.shape["occ"], mesh.shape["aux"]
    cores, xls, ys = 2, 2, naux // 2
    shape = (nocc // (cores * xls), xls, cores, ys, naux // ys)
    fine = Mesh(mesh.devices.reshape(shape), ("z", "xl", "core", "y", "xh"))
    in_specs = (P(("z", "xl", "core", "y", "xh"), None, None), P(), P(), P())
    out_specs = (P(("z", "xl", "core"), None, ("y", "xh")), P(("z", "xl", "core"), None))
    return jax.shard_map(body, mesh=fine, in_specs=in_specs, out_specs=out_specs, check_vma=False)
```

```python
import jax
import jax.numpy as jnp
from jax import lax
from jax.sharding import Mesh, PartitionSpec as P

GROUP = ("z", "xh", "xl")


def body(integrals, owner_order, occ_energy, vir_energy):
    _, _, nvir = integrals.shape
    ny, nh, nc, nl = lax.axis_size("y"), lax.axis_size("xh"), lax.axis_size("core"), lax.axis_size("xl")
    blk = nvir // (ny * nh)
    z, l, y, h, c = (lax.axis_index(a) for a in ("z", "xl", "y", "xh", "core"))
    orbital = (z * nh + h) * nl + l
    block = c * ny + y

    owner = owner_order[0]
    half = nvir // nc
    flip = [(k, k ^ 1) for k in range(nc)]
    column = lax.dynamic_index_in_dim(integrals, owner, 1, keepdims=False)
    own_half = lax.dynamic_slice_in_dim(column, c * half, half, axis=1)
    give_half = lax.dynamic_slice_in_dim(column, (1 - c) * half, half, axis=1)
    mine = jnp.stack([own_half, lax.ppermute(give_half, "core", flip)])
    mine, integrals = lax.optimization_barrier((mine, integrals))
    by_orbital = jnp.transpose(integrals, (1, 0, 2))
    panel = lax.all_gather(mine, GROUP, axis=1, tiled=True)
    panel = panel.reshape(-1, half)

    left = lax.all_to_all(by_orbital, GROUP, 0, 0, tiled=True)
    left = left.reshape(-1, nvir)
    left = jnp.concatenate([left, lax.ppermute(left, "core", flip)])

    partial_sum = lax.dot_general(
        left, panel, (((0,), (0,)), ((), ())), preferred_element_type=jnp.float32
    )
    summed = lax.psum_scatter(partial_sum, "y", scatter_dimension=1, tiled=True)

    near_energy = lax.dynamic_slice_in_dim(vir_energy, block * blk, blk)
    own_energy = lax.dynamic_index_in_dim(occ_energy, orbital, 0, keepdims=False)
    owner_energy = lax.dynamic_index_in_dim(occ_energy, owner, 0, keepdims=False)
    denominator = own_energy + owner_energy - vir_energy[:, None] - near_energy[None, :]
    part_rows = jnp.sum(summed * summed / denominator, axis=1)

    total = jnp.sum(part_rows)
    pieces = part_rows.reshape(nc, ny // 2, 2, blk)
    for bit, step, dim in ((y // 2, 2, 1), (y % 2, 1, 1)):
        keep = lax.dynamic_index_in_dim(pieces, bit, dim, keepdims=False)
        give = lax.dynamic_index_in_dim(pieces, 1 - bit, dim, keepdims=False)
        moved = [(k, k ^ step) for k in range(ny)]
        got = lax.ppermute(jnp.concatenate([give.reshape(-1), total[None]]), "y", moved)
        pieces = keep + got[:-1].reshape(keep.shape)
        total = total + got[-1]

    def index(ll, cc, yy, hh):
        return ((ll * nc + cc) * ny + yy) * nh + hh

    arrived = []
    for j in range(nc):
        moves = []
        for ll in range(nl):
            for cc in range(nc):
                for yy in range(ny):
                    for hh in range(nh):
                        x = (cc ^ j) * ny + yy
                        moves.append((index(ll, cc, yy, hh), index(hh, ll, x // nh, x % nh)))
        piece = lax.dynamic_index_in_dim(pieces, c ^ j, 0, keepdims=False)
        packed = jnp.concatenate([piece, total[None]])
        arrived.append(lax.ppermute(packed, ("xl", "core", "y", "xh"), moves))
    packed = arrived[0] + arrived[1]
    return packed[:blk].reshape(1, 1, blk), packed[blk:].reshape(1, 1)


def solution(mesh):
    nocc, naux = mesh.shape["occ"], mesh.shape["aux"]
    cores, xls, ys = 2, 2, naux // 2
    shape = (nocc // (cores * xls), xls, cores, ys, naux // ys)
    fine = Mesh(mesh.devices.reshape(shape), ("z", "xl", "core", "y", "xh"))
    in_specs = (P(("z", "xl", "core", "y", "xh"), None, None), P(), P(), P())
    out_specs = (P(("z", "xl", "core"), None, ("y", "xh")), P(("z", "xl", "core"), None))
    return jax.shard_map(body, mesh=fine, in_specs=in_specs, out_specs=out_specs, check_vma=False)
```

```python
import jax
import jax.numpy as jnp
from jax import lax
from jax.sharding import Mesh, PartitionSpec as P

GROUP = ("xh", "xl", "z")


def body(integrals, owner_order, occ_energy, vir_energy):
    _, _, nvir = integrals.shape
    ny, nh, nc, nl = lax.axis_size("y"), lax.axis_size("xh"), lax.axis_size("core"), lax.axis_size("xl")
    blk = nvir // (ny * nh)
    z, l, y, h, c = (lax.axis_index(a) for a in ("z", "xl", "y", "xh", "core"))
    nz = lax.axis_size("z")
    orbital = (h * nl + l) * nz + z
    block = c * ny + y

    owner = owner_order[0]
    half = nvir // nc
    flip = [(k, k ^ 1) for k in range(nc)]
    column = lax.dynamic_index_in_dim(integrals, owner, 1, keepdims=False)
    own_half = lax.dynamic_slice_in_dim(column, c * half, half, axis=1)
    give_half = lax.dynamic_slice_in_dim(column, (1 - c) * half, half, axis=1)
    mine = jnp.stack([own_half, lax.ppermute(give_half, "core", flip)])
    mine, integrals = lax.optimization_barrier((mine, integrals))
    by_orbital = jnp.transpose(integrals, (1, 0, 2))
    panel = lax.all_gather(mine, GROUP, axis=1, tiled=True)
    panel = panel.reshape(-1, half)

    left = lax.all_to_all(by_orbital, GROUP, 0, 0, tiled=True)
    left = left.reshape(-1, nvir)
    left = jnp.concatenate([left, lax.ppermute(left, "core", flip)])

    partial_sum = lax.dot_general(
        left, panel, (((0,), (0,)), ((), ())), preferred_element_type=jnp.float32
    )
    summed = lax.psum_scatter(partial_sum, "y", scatter_dimension=1, tiled=True)

    near_energy = lax.dynamic_slice_in_dim(vir_energy, block * blk, blk)
    own_energy = lax.dynamic_index_in_dim(occ_energy, orbital, 0, keepdims=False)
    owner_energy = lax.dynamic_index_in_dim(occ_energy, owner, 0, keepdims=False)
    denominator = own_energy + owner_energy - vir_energy[:, None] - near_energy[None, :]
    part_rows = jnp.sum(summed * summed / denominator, axis=1)

    total = jnp.sum(part_rows)
    pieces = part_rows.reshape(nc, ny // 2, 2, blk)
    for bit, step, dim in ((y // 2, 2, 1), (y % 2, 1, 1)):
        keep = lax.dynamic_index_in_dim(pieces, bit, dim, keepdims=False)
        give = lax.dynamic_index_in_dim(pieces, 1 - bit, dim, keepdims=False)
        moved = [(k, k ^ step) for k in range(ny)]
        got = lax.ppermute(jnp.concatenate([give.reshape(-1), total[None]]), "y", moved)
        pieces = keep + got[:-1].reshape(keep.shape)
        total = total + got[-1]

    def index(zz, ll, cc, yy, hh):
        return (((zz * nl + ll) * nc + cc) * ny + yy) * nh + hh

    arrived = []
    for j in range(nc):
        moves = []
        for zz in range(nz):
            for ll in range(nl):
                for cc in range(nc):
                    for yy in range(ny):
                        for hh in range(nh):
                            o = (hh * nl + ll) * nz + zz
                            x = (cc ^ j) * ny + yy
                            dest = index(o // (nl * nc), (o // nc) % nl, o % nc, x // nh, x % nh)
                            moves.append((index(zz, ll, cc, yy, hh), dest))
        piece = lax.dynamic_index_in_dim(pieces, c ^ j, 0, keepdims=False)
        packed = jnp.concatenate([piece, total[None]])
        arrived.append(lax.ppermute(packed, ("z", "xl", "core", "y", "xh"), moves))
    packed = arrived[0] + arrived[1]
    return packed[:blk].reshape(1, 1, blk), packed[blk:].reshape(1, 1)


def solution(mesh):
    nocc, naux = mesh.shape["occ"], mesh.shape["aux"]
    cores, xls, ys = 2, 2, naux // 2
    shape = (nocc // (cores * xls), xls, cores, ys, naux // ys)
    fine = Mesh(mesh.devices.reshape(shape), ("z", "xl", "core", "y", "xh"))
    in_specs = (P(("z", "xl", "core", "y", "xh"), None, None), P(), P(), P())
    out_specs = (P(("z", "xl", "core"), None, ("y", "xh")), P(("z", "xl", "core"), None))
    return jax.shard_map(body, mesh=fine, in_specs=in_specs, out_specs=out_specs, check_vma=False)
```

```python
import jax
import jax.numpy as jnp
from jax import lax
from jax.sharding import Mesh, PartitionSpec as P

GROUP = ("z", "xh", "xl")


def body(integrals, owner_order, occ_energy, vir_energy):
    _, _, nvir = integrals.shape
    ny, nh, nc, nl = lax.axis_size("y"), lax.axis_size("xh"), lax.axis_size("core"), lax.axis_size("xl")
    blk = nvir // (ny * nh)
    z, l, y, h, c = (lax.axis_index(a) for a in ("z", "xl", "y", "xh", "core"))
    orbital = (z * nh + h) * nl + l
    block = c * ny + y

    owner = owner_order[0]
    half = nvir // nc
    flip = [(k, k ^ 1) for k in range(nc)]
    column = lax.dynamic_index_in_dim(integrals, owner, 1, keepdims=False)
    own_half = lax.dynamic_slice_in_dim(column, c * half, half, axis=1)
    give_half = lax.dynamic_slice_in_dim(column, (1 - c) * half, half, axis=1)
    mine = jnp.stack([own_half, lax.ppermute(give_half, "core", flip)])
    mine, integrals = lax.optimization_barrier((mine, integrals))
    by_orbital = jnp.transpose(integrals, (1, 0, 2))
    panel = lax.all_gather(mine, GROUP, axis=1, tiled=True)
    panel = panel.reshape(-1, half)

    left = lax.all_to_all(by_orbital, GROUP, 0, 0, tiled=True)
    left = left.reshape(-1, nvir)
    left = jnp.concatenate([left, lax.ppermute(left, "core", flip)])

    partial_sum = lax.dot_general(
        left, panel, (((0,), (0,)), ((), ())), preferred_element_type=jnp.float32
    )
    summed = lax.psum_scatter(partial_sum, "y", scatter_dimension=1, tiled=True)

    near_energy = lax.dynamic_slice_in_dim(vir_energy, block * blk, blk)
    own_energy = lax.dynamic_index_in_dim(occ_energy, orbital, 0, keepdims=False)
    owner_energy = lax.dynamic_index_in_dim(occ_energy, owner, 0, keepdims=False)
    denominator = own_energy + owner_energy - vir_energy[:, None] - near_energy[None, :]
    part_rows = jnp.sum(summed * summed / denominator, axis=1)

    total = jnp.sum(part_rows)
    by_y = part_rows.reshape(nc, ny, blk)
    pieces = lax.dynamic_index_in_dim(by_y, y, 1, keepdims=False)
    sent_total = total
    for shift in range(1, ny):
        give = lax.dynamic_index_in_dim(by_y, (y + shift) % ny, 1, keepdims=False)
        moved = [(k, (k + shift) % ny) for k in range(ny)]
        got = lax.ppermute(jnp.concatenate([give.reshape(-1), sent_total[None]]), "y", moved)
        pieces = pieces + got[:-1].reshape(pieces.shape)
        total = total + got[-1]

    def index(ll, cc, yy, hh):
        return ((ll * nc + cc) * ny + yy) * nh + hh

    arrived = []
    for j in range(nc):
        moves = []
        for ll in range(nl):
            for cc in range(nc):
                for yy in range(ny):
                    for hh in range(nh):
                        x = (cc ^ j) * ny + yy
                        moves.append((index(ll, cc, yy, hh), index(hh, ll, x // nh, x % nh)))
        piece = lax.dynamic_index_in_dim(pieces, c ^ j, 0, keepdims=False)
        packed = jnp.concatenate([piece, total[None]])
        arrived.append(lax.ppermute(packed, ("xl", "core", "y", "xh"), moves))
    packed = arrived[0] + arrived[1]
    return packed[:blk].reshape(1, 1, blk), packed[blk:].reshape(1, 1)


def solution(mesh):
    nocc, naux = mesh.shape["occ"], mesh.shape["aux"]
    cores, xls, ys = 2, 2, naux // 2
    shape = (nocc // (cores * xls), xls, cores, ys, naux // ys)
    fine = Mesh(mesh.devices.reshape(shape), ("z", "xl", "core", "y", "xh"))
    in_specs = (P(("z", "xl", "core", "y", "xh"), None, None), P(), P(), P())
    out_specs = (P(("z", "xl", "core"), None, ("y", "xh")), P(("z", "xl", "core"), None))
    return jax.shard_map(body, mesh=fine, in_specs=in_specs, out_specs=out_specs, check_vma=False)
```

```python
import jax
import jax.numpy as jnp
from jax import lax
from jax.sharding import Mesh, PartitionSpec as P

GROUP = ("z", "xh", "xl")


def body(integrals, owner_order, occ_energy, vir_energy):
    _, _, nvir = integrals.shape
    ny, nh, nc, nl = lax.axis_size("y"), lax.axis_size("xh"), lax.axis_size("core"), lax.axis_size("xl")
    blk = nvir // (ny * nh)
    z, l, y, h, c = (lax.axis_index(a) for a in ("z", "xl", "y", "xh", "core"))
    orbital = (z * nh + h) * nl + l
    block = c * ny + y

    owner = owner_order[0]
    half = nvir // nc
    flip = [(k, k ^ 1) for k in range(nc)]
    column = lax.dynamic_index_in_dim(integrals, owner, 1, keepdims=False)
    own_half = lax.dynamic_slice_in_dim(column, c * half, half, axis=1)
    give_half = lax.dynamic_slice_in_dim(column, (1 - c) * half, half, axis=1)
    mine = jnp.stack([own_half, lax.ppermute(give_half, "core", flip)])
    mine, integrals = lax.optimization_barrier((mine, integrals))
    by_orbital = jnp.transpose(integrals, (1, 0, 2))
    panel = lax.all_gather(mine, GROUP, axis=1, tiled=True)
    panel = panel.reshape(-1, half)

    left = lax.all_to_all(by_orbital, GROUP, 0, 0, tiled=True)
    left = left.reshape(-1, nvir)
    left = jnp.concatenate([left, lax.ppermute(left, "core", flip)])

    partial_sum = lax.dot_general(
        left, panel, (((0,), (0,)), ((), ())), preferred_element_type=jnp.float32
    )
    summed = lax.psum_scatter(partial_sum, "y", scatter_dimension=1, tiled=True)

    near_energy = lax.dynamic_slice_in_dim(vir_energy, block * blk, blk)
    own_energy = lax.dynamic_index_in_dim(occ_energy, orbital, 0, keepdims=False)
    owner_energy = lax.dynamic_index_in_dim(occ_energy, owner, 0, keepdims=False)
    denominator = own_energy + owner_energy - vir_energy[:, None] - near_energy[None, :]
    part_rows = jnp.sum(summed * summed / denominator, axis=1)

    total = jnp.sum(part_rows)
    pieces = part_rows.reshape(ny // 2, 2, nh, blk)
    for bit, step, dim in ((y % 2, 1, 1), (y // 2, 2, 0)):
        keep = lax.dynamic_index_in_dim(pieces, bit, dim, keepdims=False)
        give = lax.dynamic_index_in_dim(pieces, 1 - bit, dim, keepdims=False)
        moved = [(k, k ^ step) for k in range(ny)]
        got = lax.ppermute(jnp.concatenate([give.reshape(-1), total[None]]), "y", moved)
        pieces = keep + got[:-1].reshape(keep.shape)
        total = total + got[-1]

    def index(ll, cc, yy, hh):
        return ((ll * nc + cc) * ny + yy) * nh + hh

    arrived = []
    for j in range(nc):
        moves = []
        for ll in range(nl):
            for cc in range(nc):
                for yy in range(ny):
                    for hh in range(nh):
                        x = yy * nh + (cc ^ j)
                        moves.append((index(ll, cc, yy, hh), index(hh, ll, x // nh, x % nh)))
        piece = lax.dynamic_index_in_dim(pieces, c ^ j, 0, keepdims=False)
        packed = jnp.concatenate([piece, total[None]])
        arrived.append(lax.ppermute(packed, ("xl", "core", "y", "xh"), moves))
    packed = arrived[0] + arrived[1]
    return packed[:blk].reshape(1, 1, blk), packed[blk:].reshape(1, 1)


def solution(mesh):
    nocc, naux = mesh.shape["occ"], mesh.shape["aux"]
    cores, xls, ys = 2, 2, naux // 2
    shape = (nocc // (cores * xls), xls, cores, ys, naux // ys)
    fine = Mesh(mesh.devices.reshape(shape), ("z", "xl", "core", "y", "xh"))
    in_specs = (P(("z", "xl", "core", "y", "xh"), None, None), P(), P(), P())
    out_specs = (P(("z", "xl", "core"), None, ("y", "xh")), P(("z", "xl", "core"), None))
    return jax.shard_map(body, mesh=fine, in_specs=in_specs, out_specs=out_specs, check_vma=False)
```
